256 devices in a mesh: dp: 16 (over y, x_hi, core), tensor: 16 (over x_lo, z).
Axes of the slice: x: 4 (x_hi: 2, x_lo: 2; x = x_hi * 2 + x_lo), y: 4, z: 8, core: 2. Of those that a mesh axis runs over, the one named last changes fastest.
Arguments:
- tokens: bfloat16 [768, 6144], P('dp', 'tensor'), may hold values from -6 to 6
- routes: int32 [768, 2], P('dp'), may hold values from 0 to 3, all different within a row; in each aligned block of 48 rows (0 to 47, 48 to 95, ...) at most 32 rows name the same one
- gate_weights: bfloat16 [768, 2], P('dp'), may hold values from 0.25 to 1
- gate_matrix: bfloat16 [16, 6144, 2048], P('dp', None, 'tensor'), may hold values from -0.078125 to 0.078125
- up_matrix: bfloat16 [16, 6144, 2048], P('dp', None, 'tensor'), may hold values from -0.078125 to 0.078125
- down_matrix: bfloat16 [16, 2048, 6144], P('dp', 'tensor'), may hold values from -0.0625 to 0.0625
- cotangent: bfloat16 [768, 6144], P('dp', 'tensor'), may hold values from -6 to 6
Outputs:
- layer_out: bfloat16 [768, 6144], P('dp', 'tensor')
- token_gradient: bfloat16 [768, 6144], P('dp', 'tensor')
- gate_gradient: bfloat16 [16, 6144, 2048], P('dp', None, 'tensor')
- up_gradient: bfloat16 [16, 6144, 2048], P('dp', None, 'tensor')
- down_gradient: bfloat16 [16, 2048, 6144], P('dp', 'tensor')
The draws below stay inside these ranges and needn't reach their ends.
Inputs may be any that keep to these rules, and one draw needn't show every extreme that they name: `routes`: within the rows of one dp index (aligned blocks of 48 rows) no expert is named by more than 32 rows, and in some such block one expert is named by exactly 32; the two experts of a row differ.
All inputs are finite; a program needn't handle non-finite values.
Results may differ from the reference program's by a relative error of at most 0.018.
Values may be sent and summed in bfloat16 or wider, within the bound.
No kernel may reach another device: no remote copies, remote signals or barrier semaphores. Data moves between devices by JAX's collectives and lax.ppermute only.
A program may use at most 128 MiB of HBM per device.

```python
import math
import jax
import jax.numpy as jnp
import numpy as np
from jax import lax

D = 6144
FFW = 8192
EXPERTS = 4
TOK_DP = 48
CAP = 32
SPAN = 4
TOKENS = 768
N_DP = 16
N_TENSOR = 16


def level_of(own_key, extent, split, low, top_value):
    level, own = 1.0, jax.random.fold_in(own_key, 6)
    for position, parts in split:
        steps = jnp.exp(jax.random.uniform(jax.random.fold_in(own, position), (parts,), jnp.float32, low / len(split), top_value / len(split)))
        level = level * jnp.repeat(steps, extent[position] // parts).reshape([-1 if axis == position else 1 for axis in range(len(extent))])
    return level


def shared_out(stream_key, own, number, rows, amount, top, reach, lean):
    ranking = jax.random.permutation(stream_key, amount)
    heavy_load, usual = load_shares(amount, rows * top, reach, lean, True), load_shares(amount, rows * top, reach, lean, False)
    places = jnp.arange(amount)

    def named(tallies, rotation):
        used = int((tallies > 0).sum())
        fixed = max(1, used // 4)
        shifted = fixed + (places - fixed + rotation * (used - fixed)) % max(1, amount - fixed)
        return jnp.zeros((amount,), jnp.int32).at[ranking[jnp.where(places < fixed, places, shifted)]].set(jnp.asarray(tallies, jnp.int32))

    tallies = jnp.where(number % 4 == 0, named(heavy_load, number // 4), named(usual, number - number // 4 - 1))
    mixed = jax.random.permutation(jax.random.fold_in(own, 3), amount)
    giver, receiver = mixed[0:amount // 2 * 2:2], mixed[1:amount // 2 * 2:2]
    room = jnp.minimum(tallies[giver] - 1, reach - tallies[receiver]) // 2
    room = jnp.where((giver == ranking[0]) | (receiver == ranking[0]) | (tallies[receiver] == 0), 0, jnp.maximum(room, 0))
    shifted = jax.random.randint(jax.random.fold_in(own, 4), (amount // 2,), 0, 1 << 20) % (room + 1)
    tallies = tallies.at[giver].add(-shifted).at[receiver].add(shifted)
    members = jnp.searchsorted(jnp.cumsum(tallies), jnp.arange(rows * top), side="right").astype(jnp.int32)
    table = members.reshape(top, rows).T
    table = table[jax.random.permutation(jax.random.fold_in(own, 1), rows)]
    rotation = jax.random.randint(jax.random.fold_in(own, 2), (rows, 1), 0, top)
    return jnp.take_along_axis(table, (jnp.arange(top)[None, :] + rotation) % top, axis=1)


def load_shares(count, total, limit, skew, full):
    portions = [(1 << 20) // math.isqrt(grade ** skew) + 1 for grade in range(1, count + 1)]
    largest = limit if full else min(limit, max(-(-total // count), total * portions[0] // sum(portions)))
    least = 1 if total - largest >= count - 1 else 0
    holding, spare = [largest] + [least] * (count - 1), total - largest - least * (count - 1)
    while spare > 0:
        candidates = [i for i in range(1, count) if holding[i] < largest] or [i for i in range(1, count) if holding[i] < limit]
        mass, budget = sum([portions[i] for i in candidates]), spare
        for i in candidates:
            addition = min(limit - holding[i], max(1, budget * portions[i] // mass), spare)
            holding[i] = holding[i] + addition
            spare = spare - addition
    return np.array(holding)


def gaussian(stream_key, dims, scale, most, shards=(), held_as=jnp.bfloat16):
    entries = jax.random.normal(stream_key, dims, jnp.float32) * scale
    if len(shards) > 0:
        entries = level_of(stream_key, dims, shards, -0.22, 0.18) * entries
    return jnp.clip(entries, min=-most, max=most).astype(held_as)


def setup_inputs(seed: int = 0) -> dict:
    splits = jax.random.split(jax.random.key(seed), 8)
    tokens = gaussian(splits[0], (TOKENS, D), 1.0, 6.0, ((0, 16), (1, 16)))
    routes_keys = jax.random.split(jax.random.fold_in(splits[1], 1), TOKENS // TOK_DP)
    routes_turns = jax.random.permutation(jax.random.fold_in(splits[1], 3), TOKENS // TOK_DP)
    routes = jax.vmap(lambda own, number: shared_out(jax.random.fold_in(splits[1], 2), own, number, TOK_DP, EXPERTS, 2, CAP, 2))(routes_keys, routes_turns).reshape((TOKENS, 2))
    gate_weights = jnp.clip(0.25 + 0.75 * jax.random.uniform(splits[2], (TOKENS, 2), jnp.float32) ** level_of(splits[2], (TOKENS, 2), ((0, 16),), -0.2, 0.2), 0.25, 1.0).astype(jnp.bfloat16)
    gate_matrix = gaussian(splits[3], (EXPERTS * SPAN, D, FFW // SPAN), D ** -0.5, 0.078125, ((0, 16), (2, 16)))
    up_matrix = gaussian(splits[4], (EXPERTS * SPAN, D, FFW // SPAN), D ** -0.5, 0.078125, ((0, 16), (2, 16)))
    down_matrix = gaussian(splits[5], (EXPERTS * SPAN, FFW // SPAN, D), FFW ** -0.5, 0.0625, ((0, 16), (1, 16)))
    cotangent = gaussian(splits[6], (TOKENS, D), 1.0, 6.0, ((0, 16), (1, 16)))
    return {"tokens": tokens, "routes": routes, "gate_weights": gate_weights, "gate_matrix": gate_matrix, "up_matrix": up_matrix, "down_matrix": down_matrix, "cotangent": cotangent}


def rounded(values):
    return lax.optimization_barrier(values.astype(jnp.bfloat16)).astype(jnp.float32)


def reference(tokens, routes, gate_weights, gate_matrix, up_matrix, down_matrix, cotangent):
    expert_span = N_DP // EXPERTS
    block_size = FFW // (expert_span * N_TENSOR)
    blocks = expert_span * N_TENSOR
    row_total = N_DP * CAP
    quarter = FFW // expert_span
    layer_sum = jnp.zeros((TOKENS, D), jnp.float32)
    token_sum = jnp.zeros((TOKENS, D), jnp.float32)
    gate_parts = []
    up_parts = []
    down_parts = []
    for expert in range(EXPERTS):
        first = expert * expert_span
        gate_full = gate_matrix[first:first + expert_span].transpose(1, 0, 2).reshape(D, FFW)
        up_full = up_matrix[first:first + expert_span].transpose(1, 0, 2).reshape(D, FFW)
        down_full = down_matrix[first:first + expert_span].reshape(FFW, D)
        hit_mask = routes == expert
        chosen = jnp.any(hit_mask, axis=1)
        row_order = jnp.argsort(jnp.where(chosen, 0, 1).astype(jnp.int32), stable=True)[:row_total].astype(jnp.int32)
        is_valid = chosen[row_order]
        weight = jnp.sum(jnp.where(hit_mask, gate_weights.astype(jnp.float32), jnp.float32(0.0)), axis=1)[row_order]
        weight = jnp.where(is_valid, weight, jnp.float32(0.0))
        picked = jnp.where(is_valid[:, None], tokens[row_order], jnp.zeros((), jnp.bfloat16))
        slot_grad = (weight[:, None] * cotangent[row_order].astype(jnp.float32)).astype(jnp.bfloat16)
        gate_pre = jnp.dot(picked, gate_full, preferred_element_type=jnp.float32)
        up_pre = jnp.dot(picked, up_full, preferred_element_type=jnp.float32)
        sigmoid_gate = jax.nn.sigmoid(gate_pre)
        activated = gate_pre * sigmoid_gate
        hidden = (activated * up_pre).astype(jnp.bfloat16)
        hidden_grad = jnp.dot(slot_grad, down_full.T, preferred_element_type=jnp.float32)
        gate_grad = (hidden_grad * up_pre * sigmoid_gate * (1.0 + gate_pre * (1.0 - sigmoid_gate))).astype(jnp.bfloat16)
        up_grad = (hidden_grad * activated).astype(jnp.bfloat16)

        def add_block(block_index, totals):
            out_total, back_total = totals
            offset = (block_index * block_size).astype(jnp.int32)
            hidden_block = lax.dynamic_slice_in_dim(hidden, offset, block_size, 1)
            ggrad_block = lax.dynamic_slice_in_dim(gate_grad, offset, block_size, 1)
            ugrad_block = lax.dynamic_slice_in_dim(up_grad, offset, block_size, 1)
            down_block = lax.dynamic_slice_in_dim(down_full, offset, block_size, 0)
            gate_block = lax.dynamic_slice_in_dim(gate_full, offset, block_size, 1)
            up_block = lax.dynamic_slice_in_dim(up_full, offset, block_size, 1)
            out_total = out_total + rounded(jnp.dot(hidden_block, down_block, preferred_element_type=jnp.float32))
            back_term = jnp.dot(ggrad_block, gate_block.T, preferred_element_type=jnp.float32) + jnp.dot(ugrad_block, up_block.T, preferred_element_type=jnp.float32)
            back_total = back_total + rounded(back_term)
            return out_total, back_total

        zeros_init = jnp.zeros((row_total, D), jnp.float32)
        out_total, back_total = lax.fori_loop(0, blocks, add_block, (zeros_init, zeros_init))
        layer_sum = layer_sum.at[row_order].add(weight[:, None] * out_total)
        token_sum = token_sum.at[row_order].add(jnp.where(is_valid[:, None], back_total, jnp.float32(0.0)))
        gate_grad_full = jnp.dot(picked.T, gate_grad, preferred_element_type=jnp.float32).astype(jnp.bfloat16)
        up_grad_full = jnp.dot(picked.T, up_grad, preferred_element_type=jnp.float32).astype(jnp.bfloat16)
        down_grad_full = jnp.dot(hidden.T, slot_grad, preferred_element_type=jnp.float32).astype(jnp.bfloat16)
        gate_parts.append(gate_grad_full.reshape(D, expert_span, quarter).transpose(1, 0, 2))
        up_parts.append(up_grad_full.reshape(D, expert_span, quarter).transpose(1, 0, 2))
        down_parts.append(down_grad_full.reshape(expert_span, quarter, D))
    return (layer_sum.astype(jnp.bfloat16), token_sum.astype(jnp.bfloat16), jnp.concatenate(gate_parts, 0), jnp.concatenate(up_parts, 0), jnp.concatenate(down_parts, 0))
```

```python
import jax
import jax.numpy as jnp
from jax import lax
from jax.sharding import PartitionSpec as P

EXPERTS = 4
CAP = 32


precise = lax.Precision.HIGHEST


def slot_tables(routes, gate_weights, capacity):
    experts = jnp.arange(EXPERTS, dtype=jnp.int32)
    hit_mask = routes[:, :, None] == experts[None, None, :]
    chosen = jnp.any(hit_mask, axis=1)
    weights = jnp.sum(
        jnp.where(hit_mask, gate_weights.astype(jnp.float32)[:, :, None], jnp.float32(0.0)), axis=1
    )
    places = jnp.cumsum(chosen.astype(jnp.int32), axis=0) - 1
    columns = jnp.arange(capacity, dtype=jnp.int32)
    onehot = (places[:, :, None] == columns[None, None, :]) & chosen[:, :, None]
    return (onehot, weights)


def per_device(tokens, routes, gate_weights, gate_matrix, up_matrix, down_matrix, cotangent):
    feature_cols = tokens.shape[1]
    n_dp = lax.axis_size("dp")
    expert_span = n_dp // EXPERTS
    half = n_dp // 2
    core = lax.axis_index("dp") % 2
    pair = [(d, d ^ 1) for d in range(n_dp)]
    onehot, weights = slot_tables(routes, gate_weights, CAP)
    member = onehot.astype(jnp.float32)
    scaled = member * weights[:, :, None]

    def spread(slot_table):
        widened = jnp.broadcast_to(
            slot_table[:, :, None, :], (slot_table.shape[0], EXPERTS, expert_span, CAP)
        )
        return widened.reshape(slot_table.shape[0], EXPERTS * expert_span * CAP)

    member_wide = spread(member)
    scaled_wide = spread(scaled)
    token_send = jnp.einsum(
        "tr,tc->rc", member_wide.astype(jnp.bfloat16), tokens, preferred_element_type=jnp.float32
    ).astype(jnp.bfloat16)
    grad_send = jnp.einsum(
        "tr,tc->rc", scaled_wide, cotangent.astype(jnp.float32), precision=precise
    ).astype(jnp.bfloat16)
    send = jnp.concatenate(
        [token_send.reshape(n_dp, CAP, feature_cols), grad_send.reshape(n_dp, CAP, feature_cols)],
        axis=1,
    )
    recv = lax.all_to_all(send, "dp", split_axis=0, concat_axis=0, tiled=True)
    mine = lax.dynamic_slice_in_dim(recv, core * half, half, axis=0)
    mine = mine.reshape(half, 2, CAP, feature_cols).transpose(1, 0, 2, 3)
    mine = mine.reshape(2, half * CAP, feature_cols)
    mine_full = lax.all_gather(mine, "tensor", axis=2, tiled=True)
    other_full = lax.ppermute(mine_full, "dp", pair)

    gate_local = gate_matrix[0]
    up_local = up_matrix[0]
    down_local = down_matrix[0]

    def forward(rows):
        gate_pre = jnp.dot(rows, gate_local, preferred_element_type=jnp.float32)
        up_pre = jnp.dot(rows, up_local, preferred_element_type=jnp.float32)
        sigmoid_gate = jax.nn.sigmoid(gate_pre)
        activated = gate_pre * sigmoid_gate
        hidden = (activated * up_pre).astype(jnp.bfloat16)
        out_t = jnp.einsum(
            "hd,rh->dr", down_local, hidden, preferred_element_type=jnp.float32
        ).astype(jnp.bfloat16)
        return gate_pre, up_pre, sigmoid_gate, activated, hidden, out_t

    def backward(rows, grads, gate_pre, up_pre, sigmoid_gate, activated):
        hidden_grad = jnp.einsum(
            "rd,hd->rh", grads, down_local, preferred_element_type=jnp.float32
        )
        gate_grad = (
            hidden_grad * up_pre * sigmoid_gate * (1.0 + gate_pre * (1.0 - sigmoid_gate))
        ).astype(jnp.bfloat16)
        up_grad = (hidden_grad * activated).astype(jnp.bfloat16)
        back_t = (
            jnp.einsum("dh,rh->dr", gate_local, gate_grad, preferred_element_type=jnp.float32)
            + jnp.einsum("dh,rh->dr", up_local, up_grad, preferred_element_type=jnp.float32)
        ).astype(jnp.bfloat16)
        return gate_grad, up_grad, back_t

    rows_a, grads_a = mine_full[0], mine_full[1]
    rows_b, grads_b = other_full[0], other_full[1]
    fa = forward(rows_a)
    fb = forward(rows_b)

    def combine(own_t, partner_t):
        summed = own_t.astype(jnp.float32) + partner_t.astype(jnp.float32)
        scattered = lax.psum_scatter(
            summed.astype(jnp.bfloat16), "tensor", scatter_dimension=0, tiled=True
        )
        return scattered.T

    out_partner = lax.ppermute(fb[5], "dp", pair)
    out_rows = combine(fa[5], out_partner)

    ga, ua, back_a = backward(rows_a, grads_a, *fa[:4])
    gb, ub, back_b = backward(rows_b, grads_b, *fb[:4])
    back_partner = lax.ppermute(back_b, "dp", pair)
    back_rows = combine(back_a, back_partner)

    gate_gradient = (
        jnp.einsum("rd,rh->dh", rows_a, ga, preferred_element_type=jnp.float32)
        + jnp.einsum("rd,rh->dh", rows_b, gb, preferred_element_type=jnp.float32)
    ).astype(jnp.bfloat16)[None]
    up_gradient = (
        jnp.einsum("rd,rh->dh", rows_a, ua, preferred_element_type=jnp.float32)
        + jnp.einsum("rd,rh->dh", rows_b, ub, preferred_element_type=jnp.float32)
    ).astype(jnp.bfloat16)[None]
    down_gradient = (
        jnp.einsum("rh,rd->hd", fa[4], grads_a, preferred_element_type=jnp.float32)
        + jnp.einsum("rh,rd->hd", fb[4], grads_b, preferred_element_type=jnp.float32)
    ).astype(jnp.bfloat16)[None]

    done = jnp.concatenate(
        [
            out_rows.reshape(half, CAP, feature_cols),
            back_rows.reshape(half, CAP, feature_cols),
        ],
        axis=1,
    )
    ret_send = lax.dynamic_update_slice_in_dim(
        jnp.zeros((n_dp, 2 * CAP, feature_cols), jnp.bfloat16), done, core * half, axis=0
    )
    returned = lax.all_to_all(ret_send, "dp", split_axis=0, concat_axis=0, tiled=True).astype(
        jnp.float32
    )
    returned_out = returned[:, :CAP].reshape(-1, feature_cols)
    returned_back = returned[:, CAP:].reshape(-1, feature_cols)
    layer_out = jnp.dot(
        scaled_wide, returned_out, precision=precise, preferred_element_type=jnp.float32
    ).astype(jnp.bfloat16)
    token_gradient = jnp.dot(
        member_wide, returned_back, precision=precise, preferred_element_type=jnp.float32
    ).astype(jnp.bfloat16)
    return (layer_out, token_gradient, gate_gradient, up_gradient, down_gradient)


def solution(mesh):
    in_specs = (
        P("dp", "tensor"),
        P("dp", None),
        P("dp", None),
        P("dp", None, "tensor"),
        P("dp", None, "tensor"),
        P("dp", "tensor", None),
        P("dp", "tensor"),
    )
    out_specs = (
        P("dp", "tensor"),
        P("dp", "tensor"),
        P("dp", None, "tensor"),
        P("dp", None, "tensor"),
        P("dp", "tensor", None),
    )
    return jax.shard_map(
        per_device, mesh=mesh, in_specs=in_specs, out_specs=out_specs, check_vma=False
    )
```

```python
import jax
import jax.numpy as jnp
from jax import lax
from jax.sharding import PartitionSpec as P

EXPERTS = 4
CAP = 32


precise = lax.Precision.HIGHEST


def slot_tables(routes, gate_weights, capacity):
    experts = jnp.arange(EXPERTS, dtype=jnp.int32)
    hit_mask = routes[:, :, None] == experts[None, None, :]
    chosen = jnp.any(hit_mask, axis=1)
    weights = jnp.sum(
        jnp.where(hit_mask, gate_weights.astype(jnp.float32)[:, :, None], jnp.float32(0.0)), axis=1
    )
    places = jnp.cumsum(chosen.astype(jnp.int32), axis=0) - 1
    columns = jnp.arange(capacity, dtype=jnp.int32)
    onehot = (places[:, :, None] == columns[None, None, :]) & chosen[:, :, None]
    return (onehot, weights)


def per_device(tokens, routes, gate_weights, gate_matrix, up_matrix, down_matrix, cotangent):
    feature_cols = tokens.shape[1]
    n_dp = lax.axis_size("dp")
    expert_span = n_dp // EXPERTS
    half = n_dp // 2
    core = lax.axis_index("dp") % 2
    pair = [(d, d ^ 1) for d in range(n_dp)]
    onehot, weights = slot_tables(routes, gate_weights, CAP)
    member = onehot.astype(jnp.float32)
    scaled = member * weights[:, :, None]

    def spread(slot_table):
        widened = jnp.broadcast_to(
            slot_table[:, :, None, :], (slot_table.shape[0], EXPERTS, expert_span, CAP)
        )
        return widened.reshape(slot_table.shape[0], EXPERTS * expert_span * CAP)

    member_wide = spread(member)
    scaled_wide = spread(scaled)
    token_send = jnp.einsum(
        "tr,tc->rc", member_wide.astype(jnp.bfloat16), tokens, preferred_element_type=jnp.float32
    ).astype(jnp.bfloat16)
    grad_send = jnp.einsum(
        "tr,tc->rc", scaled_wide, cotangent.astype(jnp.float32), precision=precise
    ).astype(jnp.bfloat16)
    send = jnp.concatenate(
        [token_send.reshape(n_dp, CAP, feature_cols), grad_send.reshape(n_dp, CAP, feature_cols)],
        axis=1,
    )
    recv = lax.all_to_all(send, "dp", split_axis=0, concat_axis=0, tiled=True)
    mine = lax.dynamic_slice_in_dim(recv, core * half, half, axis=0)
    mine = mine.reshape(half, 2, CAP, feature_cols).transpose(1, 0, 2, 3)
    mine = mine.reshape(2, half * CAP, feature_cols)
    mine_full = lax.all_gather(mine, "tensor", axis=2, tiled=True)
    other_full = lax.ppermute(mine_full, "dp", pair)

    gate_local = gate_matrix[0]
    up_local = up_matrix[0]
    down_local = down_matrix[0]

    def forward(rows):
        gate_pre = jnp.dot(rows, gate_local, preferred_element_type=jnp.float32)
        up_pre = jnp.dot(rows, up_local, preferred_element_type=jnp.float32)
        sigmoid_gate = jax.nn.sigmoid(gate_pre)
        activated = gate_pre * sigmoid_gate
        hidden = (activated * up_pre).astype(jnp.bfloat16)
        out_t = jnp.einsum(
            "hd,rh->dr", down_local, hidden, preferred_element_type=jnp.float32
        ).astype(jnp.bfloat16)
        return gate_pre, up_pre, sigmoid_gate, activated, hidden, out_t

    def backward(rows, grads, gate_pre, up_pre, sigmoid_gate, activated):
        hidden_grad = jnp.einsum(
            "rd,hd->rh", grads, down_local, preferred_element_type=jnp.float32
        )
        gate_grad = (
            hidden_grad * up_pre * sigmoid_gate * (1.0 + gate_pre * (1.0 - sigmoid_gate))
        ).astype(jnp.bfloat16)
        up_grad = (hidden_grad * activated).astype(jnp.bfloat16)
        back_t = (
            jnp.einsum("dh,rh->dr", gate_local, gate_grad, preferred_element_type=jnp.float32)
            + jnp.einsum("dh,rh->dr", up_local, up_grad, preferred_element_type=jnp.float32)
        ).astype(jnp.bfloat16)
        return gate_grad, up_grad, back_t

    rows_a, grads_a = mine_full[0], mine_full[1]
    rows_b, grads_b = other_full[0], other_full[1]
    fa = forward(rows_a)
    fb = forward(rows_b)

    ga, ua, back_a = backward(rows_a, grads_a, *fa[:4])
    gb, ub, back_b = backward(rows_b, grads_b, *fb[:4])
    partner = lax.ppermute(jnp.stack([fb[5], back_b]), "dp", pair)
    own = jnp.stack([fa[5], back_a], axis=1)
    summed = own.astype(jnp.float32) + partner.transpose(1, 0, 2).astype(jnp.float32)
    summed = summed.astype(jnp.bfloat16).reshape(own.shape[0], -1)
    scattered = lax.psum_scatter(summed, "tensor", scatter_dimension=0, tiled=True)
    scattered = scattered.reshape(scattered.shape[0], 2, -1)
    out_rows = scattered[:, 0].T
    back_rows = scattered[:, 1].T

    gate_gradient = (
        jnp.einsum("rd,rh->dh", rows_a, ga, preferred_element_type=jnp.float32)
        + jnp.einsum("rd,rh->dh", rows_b, gb, preferred_element_type=jnp.float32)
    ).astype(jnp.bfloat16)[None]
    up_gradient = (
        jnp.einsum("rd,rh->dh", rows_a, ua, preferred_element_type=jnp.float32)
        + jnp.einsum("rd,rh->dh", rows_b, ub, preferred_element_type=jnp.float32)
    ).astype(jnp.bfloat16)[None]
    down_gradient = (
        jnp.einsum("rh,rd->hd", fa[4], grads_a, preferred_element_type=jnp.float32)
        + jnp.einsum("rh,rd->hd", fb[4], grads_b, preferred_element_type=jnp.float32)
    ).astype(jnp.bfloat16)[None]

    done = jnp.concatenate(
        [
            out_rows.reshape(half, CAP, feature_cols),
            back_rows.reshape(half, CAP, feature_cols),
        ],
        axis=1,
    )
    ret_send = lax.dynamic_update_slice_in_dim(
        jnp.zeros((n_dp, 2 * CAP, feature_cols), jnp.bfloat16), done, core * half, axis=0
    )
    returned = lax.all_to_all(ret_send, "dp", split_axis=0, concat_axis=0, tiled=True).astype(
        jnp.float32
    )
    returned_out = returned[:, :CAP].reshape(-1, feature_cols)
    returned_back = returned[:, CAP:].reshape(-1, feature_cols)
    layer_out = jnp.dot(
        scaled_wide, returned_out, precision=precise, preferred_element_type=jnp.float32
    ).astype(jnp.bfloat16)
    token_gradient = jnp.dot(
        member_wide, returned_back, precision=precise, preferred_element_type=jnp.float32
    ).astype(jnp.bfloat16)
    return (layer_out, token_gradient, gate_gradient, up_gradient, down_gradient)


def solution(mesh):
    in_specs = (
        P("dp", "tensor"),
        P("dp", None),
        P("dp", None),
        P("dp", None, "tensor"),
        P("dp", None, "tensor"),
        P("dp", "tensor", None),
        P("dp", "tensor"),
    )
    out_specs = (
        P("dp", "tensor"),
        P("dp", "tensor"),
        P("dp", None, "tensor"),
        P("dp", None, "tensor"),
        P("dp", "tensor", None),
    )
    return jax.shard_map(
        per_device, mesh=mesh, in_specs=in_specs, out_specs=out_specs, check_vma=False
    )
```

```python
import jax
import jax.numpy as jnp
from jax import lax
from jax.sharding import Mesh, NamedSharding, PartitionSpec as P

EXPERTS = 4
CAP = 32
DP = ("y", "xhi", "core")
TN = ("xlo", "z")
SRC = ("y", "xhi")


precise = lax.Precision.HIGHEST


def slot_tables(routes, gate_weights, capacity):
    experts = jnp.arange(EXPERTS, dtype=jnp.int32)
    hit_mask = routes[:, :, None] == experts[None, None, :]
    chosen = jnp.any(hit_mask, axis=1)
    weights = jnp.sum(
        jnp.where(hit_mask, gate_weights.astype(jnp.float32)[:, :, None], jnp.float32(0.0)), axis=1
    )
    places = jnp.cumsum(chosen.astype(jnp.int32), axis=0) - 1
    columns = jnp.arange(capacity, dtype=jnp.int32)
    onehot = (places[:, :, None] == columns[None, None, :]) & chosen[:, :, None]
    return (onehot, weights)


def per_device(tokens, routes, gate_weights, gate_matrix, up_matrix, down_matrix, cotangent):
    feature_cols = tokens.shape[1]
    n_src = lax.axis_size(SRC)
    expert_span = n_src // EXPERTS
    onehot, weights = slot_tables(routes, gate_weights, CAP)
    member = onehot.astype(jnp.float32)
    scaled = member * weights[:, :, None]

    def spread(slot_table):
        widened = jnp.broadcast_to(
            slot_table[:, :, None, :], (slot_table.shape[0], EXPERTS, expert_span, CAP)
        )
        return widened.reshape(slot_table.shape[0], EXPERTS * expert_span * CAP)

    member_wide = spread(member)
    scaled_wide = spread(scaled)
    token_send = jnp.einsum(
        "tr,tc->rc", member_wide.astype(jnp.bfloat16), tokens, preferred_element_type=jnp.float32
    ).astype(jnp.bfloat16)
    grad_send = jnp.einsum(
        "tr,tc->rc", scaled_wide, cotangent.astype(jnp.float32), precision=precise
    ).astype(jnp.bfloat16)
    send = jnp.concatenate(
        [token_send.reshape(n_src, CAP, feature_cols), grad_send.reshape(n_src, CAP, feature_cols)],
        axis=1,
    )
    recv = lax.all_to_all(send, SRC, split_axis=0, concat_axis=0, tiled=True)
    mine = recv.reshape(n_src, 2, CAP, feature_cols).transpose(1, 0, 2, 3)
    mine = mine.reshape(2, n_src * CAP, feature_cols)
    mine_full = lax.all_gather(mine, TN, axis=2, tiled=True)
    pair = [(0, 1), (1, 0)]
    other_full = lax.ppermute(mine_full, "core", pair)

    gate_local = gate_matrix[0]
    up_local = up_matrix[0]
    down_local = down_matrix[0]

    def forward(rows):
        gate_pre = jnp.dot(rows, gate_local, preferred_element_type=jnp.float32)
        up_pre = jnp.dot(rows, up_local, preferred_element_type=jnp.float32)
        sigmoid_gate = jax.nn.sigmoid(gate_pre)
        activated = gate_pre * sigmoid_gate
        hidden = (activated * up_pre).astype(jnp.bfloat16)
        out_t = jnp.einsum(
            "hd,rh->dr", down_local, hidden, preferred_element_type=jnp.float32
        ).astype(jnp.bfloat16)
        return gate_pre, up_pre, sigmoid_gate, activated, hidden, out_t

    def backward(rows, grads, gate_pre, up_pre, sigmoid_gate, activated):
        hidden_grad = jnp.einsum(
            "rd,hd->rh", grads, down_local, preferred_element_type=jnp.float32
        )
        gate_grad = (
            hidden_grad * up_pre * sigmoid_gate * (1.0 + gate_pre * (1.0 - sigmoid_gate))
        ).astype(jnp.bfloat16)
        up_grad = (hidden_grad * activated).astype(jnp.bfloat16)
        back_t = (
            jnp.einsum("dh,rh->dr", gate_local, gate_grad, preferred_element_type=jnp.float32)
            + jnp.einsum("dh,rh->dr", up_local, up_grad, preferred_element_type=jnp.float32)
        ).astype(jnp.bfloat16)
        return gate_grad, up_grad, back_t

    rows_a, grads_a = mine_full[0], mine_full[1]
    rows_b, grads_b = other_full[0], other_full[1]
    fa = forward(rows_a)
    fb = forward(rows_b)

    ga, ua, back_a = backward(rows_a, grads_a, *fa[:4])
    gb, ub, back_b = backward(rows_b, grads_b, *fb[:4])
    partner = lax.ppermute(jnp.concatenate([fb[5], back_b], axis=1), "core", pair)
    own = jnp.concatenate([fa[5], back_a], axis=1)
    summed = (own.astype(jnp.float32) + partner.astype(jnp.float32)).astype(jnp.bfloat16)
    scattered = lax.psum_scatter(summed, TN, scatter_dimension=0, tiled=True)
    n_rows = fa[5].shape[1]
    out_rows = scattered[:, :n_rows].T
    back_rows = scattered[:, n_rows:].T

    gate_gradient = (
        jnp.einsum("rd,rh->dh", rows_a, ga, preferred_element_type=jnp.float32)
        + jnp.einsum("rd,rh->dh", rows_b, gb, preferred_element_type=jnp.float32)
    ).astype(jnp.bfloat16)[None]
    up_gradient = (
        jnp.einsum("rd,rh->dh", rows_a, ua, preferred_element_type=jnp.float32)
        + jnp.einsum("rd,rh->dh", rows_b, ub, preferred_element_type=jnp.float32)
    ).astype(jnp.bfloat16)[None]
    down_gradient = (
        jnp.einsum("rh,rd->hd", fa[4], grads_a, preferred_element_type=jnp.float32)
        + jnp.einsum("rh,rd->hd", fb[4], grads_b, preferred_element_type=jnp.float32)
    ).astype(jnp.bfloat16)[None]

    done = jnp.concatenate(
        [
            out_rows.reshape(n_src, CAP, feature_cols),
            back_rows.reshape(n_src, CAP, feature_cols),
        ],
        axis=1,
    )
    returned = lax.all_to_all(done, SRC, split_axis=0, concat_axis=0, tiled=True).astype(
        jnp.float32
    )
    returned_out = returned[:, :CAP].reshape(-1, feature_cols)
    returned_back = returned[:, CAP:].reshape(-1, feature_cols)
    layer_out = jnp.dot(
        scaled_wide, returned_out, precision=precise, preferred_element_type=jnp.float32
    ).astype(jnp.bfloat16)
    token_gradient = jnp.dot(
        member_wide, returned_back, precision=precise, preferred_element_type=jnp.float32
    ).astype(jnp.bfloat16)
    return (layer_out, token_gradient, gate_gradient, up_gradient, down_gradient)


def solution(mesh):
    sizes = dict(mesh.shape)
    sub = Mesh(
        mesh.devices.reshape(
            sizes["dp"] // 4, 2, 2, 2, sizes["tensor"] // 2
        ),
        DP + TN,
    )
    in_specs = (
        P(DP, TN),
        P(DP, None),
        P(DP, None),
        P(DP, None, TN),
        P(DP, None, TN),
        P(DP, TN, None),
        P(DP, TN),
    )
    out_specs = (
        P(DP, TN),
        P(DP, TN),
        P(DP, None, TN),
        P(DP, None, TN),
        P(DP, TN, None),
    )
    placed = (
        P("dp", "tensor"),
        P("dp", "tensor"),
        P("dp", None, "tensor"),
        P("dp", None, "tensor"),
        P("dp", "tensor", None),
    )
    inner = jax.shard_map(
        per_device, mesh=sub, in_specs=in_specs, out_specs=out_specs, check_vma=False
    )

    def run(*args):
        outs = inner(*args)
        return tuple(
            lax.with_sharding_constraint(o, NamedSharding(mesh, p)) for o, p in zip(outs, placed)
        )

    return run
```

```python
import jax
import jax.numpy as jnp
from jax import lax
from jax.experimental.layout import Layout, with_layout_constraint
from jax.sharding import Mesh, NamedSharding, PartitionSpec as P

EXPERTS = 4
CAP = 32
DP = ("y", "xhi", "core")
TN = ("xlo", "z")
SRC = ("y", "xhi")


precise = lax.Precision.HIGHEST


def slot_tables(routes, gate_weights, capacity):
    experts = jnp.arange(EXPERTS, dtype=jnp.int32)
    hit_mask = routes[:, :, None] == experts[None, None, :]
    chosen = jnp.any(hit_mask, axis=1)
    weights = jnp.sum(
        jnp.where(hit_mask, gate_weights.astype(jnp.float32)[:, :, None], jnp.float32(0.0)), axis=1
    )
    places = jnp.cumsum(chosen.astype(jnp.int32), axis=0) - 1
    columns = jnp.arange(capacity, dtype=jnp.int32)
    onehot = (places[:, :, None] == columns[None, None, :]) & chosen[:, :, None]
    return (onehot, weights)


def per_device(tokens, routes, gate_weights, gate_matrix, up_matrix, down_matrix, cotangent):
    feature_cols = tokens.shape[1]
    n_src = lax.axis_size(SRC)
    expert_span = n_src // EXPERTS
    onehot, weights = slot_tables(routes, gate_weights, CAP)
    member = onehot.astype(jnp.float32)
    scaled = member * weights[:, :, None]

    def spread(slot_table):
        widened = jnp.broadcast_to(
            slot_table[:, :, None, :], (slot_table.shape[0], EXPERTS, expert_span, CAP)
        )
        return widened.reshape(slot_table.shape[0], EXPERTS * expert_span * CAP)

    member_wide = spread(member)
    scaled_wide = spread(scaled)
    token_send = jnp.einsum(
        "tr,tc->rc", member_wide.astype(jnp.bfloat16), tokens, preferred_element_type=jnp.float32
    ).astype(jnp.bfloat16)
    grad_send = jnp.einsum(
        "tr,tc->rc", scaled_wide, cotangent.astype(jnp.float32), precision=precise
    ).astype(jnp.bfloat16)
    send = jnp.concatenate(
        [token_send.reshape(n_src, CAP, feature_cols), grad_send.reshape(n_src, CAP, feature_cols)],
        axis=1,
    )
    recv = lax.all_to_all(send, SRC, split_axis=0, concat_axis=0, tiled=True)
    mine = recv.reshape(n_src, 2, CAP, feature_cols).transpose(1, 0, 2, 3)
    mine = mine.reshape(2, n_src * CAP, feature_cols)
    mine_full = lax.all_gather(mine, TN, axis=2, tiled=True)
    pair = [(0, 1), (1, 0)]
    other_full = lax.ppermute(mine_full, "core", pair)

    gate_local = gate_matrix[0]
    up_local = up_matrix[0]
    down_local = down_matrix[0]

    def forward(rows):
        gate_pre = jnp.dot(rows, gate_local, preferred_element_type=jnp.float32)
        up_pre = jnp.dot(rows, up_local, preferred_element_type=jnp.float32)
        sigmoid_gate = jax.nn.sigmoid(gate_pre)
        activated = gate_pre * sigmoid_gate
        hidden = (activated * up_pre).astype(jnp.bfloat16)
        out_t = jnp.einsum(
            "hd,rh->dr", down_local, hidden, preferred_element_type=jnp.float32
        ).astype(jnp.bfloat16)
        out_t = with_layout_constraint(out_t, Layout(major_to_minor=(0, 1)))
        return gate_pre, up_pre, sigmoid_gate, activated, hidden, out_t

    def backward(rows, grads, gate_pre, up_pre, sigmoid_gate, activated):
        hidden_grad = jnp.einsum(
            "rd,hd->rh", grads, down_local, preferred_element_type=jnp.float32
        )
        gate_grad = (
            hidden_grad * up_pre * sigmoid_gate * (1.0 + gate_pre * (1.0 - sigmoid_gate))
        ).astype(jnp.bfloat16)
        up_grad = (hidden_grad * activated).astype(jnp.bfloat16)
        back_t = (
            jnp.einsum("dh,rh->dr", gate_local, gate_grad, preferred_element_type=jnp.float32)
            + jnp.einsum("dh,rh->dr", up_local, up_grad, preferred_element_type=jnp.float32)
        ).astype(jnp.bfloat16)
        back_t = with_layout_constraint(back_t, Layout(major_to_minor=(0, 1)))
        return gate_grad, up_grad, back_t

    rows_a, grads_a = mine_full[0], mine_full[1]
    rows_b, grads_b = other_full[0], other_full[1]
    fa = forward(rows_a)
    fb = forward(rows_b)

    ga, ua, back_a = backward(rows_a, grads_a, *fa[:4])
    gb, ub, back_b = backward(rows_b, grads_b, *fb[:4])
    partner = lax.ppermute(jnp.concatenate([fb[5], back_b], axis=1), "core", pair)
    own = jnp.concatenate([fa[5], back_a], axis=1)
    summed = (own.astype(jnp.float32) + partner.astype(jnp.float32)).astype(jnp.bfloat16)
    scattered = lax.psum_scatter(summed, TN, scatter_dimension=0, tiled=True)
    n_rows = fa[5].shape[1]
    out_rows = scattered[:, :n_rows].T
    back_rows = scattered[:, n_rows:].T

    gate_gradient = (
        jnp.einsum("rd,rh->dh", rows_a, ga, preferred_element_type=jnp.float32)
        + jnp.einsum("rd,rh->dh", rows_b, gb, preferred_element_type=jnp.float32)
    ).astype(jnp.bfloat16)[None]
    up_gradient = (
        jnp.einsum("rd,rh->dh", rows_a, ua, preferred_element_type=jnp.float32)
        + jnp.einsum("rd,rh->dh", rows_b, ub, preferred_element_type=jnp.float32)
    ).astype(jnp.bfloat16)[None]
    down_gradient = (
        jnp.einsum("rh,rd->hd", fa[4], grads_a, preferred_element_type=jnp.float32)
        + jnp.einsum("rh,rd->hd", fb[4], grads_b, preferred_element_type=jnp.float32)
    ).astype(jnp.bfloat16)[None]

    done = jnp.concatenate(
        [
            out_rows.reshape(n_src, CAP, feature_cols),
            back_rows.reshape(n_src, CAP, feature_cols),
        ],
        axis=1,
    )
    returned = lax.all_to_all(done, SRC, split_axis=0, concat_axis=0, tiled=True).astype(
        jnp.float32
    )
    returned_out = returned[:, :CAP].reshape(-1, feature_cols)
    returned_back = returned[:, CAP:].reshape(-1, feature_cols)
    layer_out = jnp.dot(
        scaled_wide, returned_out, precision=precise, preferred_element_type=jnp.float32
    ).astype(jnp.bfloat16)
    token_gradient = jnp.dot(
        member_wide, returned_back, precision=precise, preferred_element_type=jnp.float32
    ).astype(jnp.bfloat16)
    return (layer_out, token_gradient, gate_gradient, up_gradient, down_gradient)


def solution(mesh):
    sizes = dict(mesh.shape)
    sub = Mesh(
        mesh.devices.reshape(
            sizes["dp"] // 4, 2, 2, 2, sizes["tensor"] // 2
        ),
        DP + TN,
    )
    in_specs = (
        P(DP, TN),
        P(DP, None),
        P(DP, None),
        P(DP, None, TN),
        P(DP, None, TN),
        P(DP, TN, None),
        P(DP, TN),
    )
    out_specs = (
        P(DP, TN),
        P(DP, TN),
        P(DP, None, TN),
        P(DP, None, TN),
        P(DP, TN, None),
    )
    placed = (
        P("dp", "tensor"),
        P("dp", "tensor"),
        P("dp", None, "tensor"),
        P("dp", None, "tensor"),
        P("dp", "tensor", None),
    )
    inner = jax.shard_map(
        per_device, mesh=sub, in_specs=in_specs, out_specs=out_specs, check_vma=False
    )

    def run(*args):
        outs = inner(*args)
        return tuple(
            lax.with_sharding_constraint(o, NamedSharding(mesh, p)) for o, p in zip(outs, placed)
        )

    return run
```

```python
import jax
import jax.numpy as jnp
from jax import lax
from jax.experimental.layout import Layout, with_layout_constraint
from jax.sharding import Mesh, NamedSharding, PartitionSpec as P

EXPERTS = 4
CAP = 32
DP = ("y", "xhi", "core")
TN = ("xlo", "z")
SRC = ("y", "xhi")


precise = lax.Precision.HIGHEST


def slot_tables(routes, gate_weights, capacity):
    experts = jnp.arange(EXPERTS, dtype=jnp.int32)
    hit_mask = routes[:, :, None] == experts[None, None, :]
    chosen = jnp.any(hit_mask, axis=1)
    weights = jnp.sum(
        jnp.where(hit_mask, gate_weights.astype(jnp.float32)[:, :, None], jnp.float32(0.0)), axis=1
    )
    places = jnp.cumsum(chosen.astype(jnp.int32), axis=0) - 1
    columns = jnp.arange(capacity, dtype=jnp.int32)
    onehot = (places[:, :, None] == columns[None, None, :]) & chosen[:, :, None]
    return (onehot, weights)


def per_device(tokens, routes, gate_weights, gate_matrix, up_matrix, down_matrix, cotangent):
    feature_cols = tokens.shape[1]
    n_src = lax.axis_size(SRC)
    expert_span = n_src // EXPERTS
    onehot, weights = slot_tables(routes, gate_weights, CAP)
    member = onehot.astype(jnp.float32)
    scaled = member * weights[:, :, None]

    def spread(slot_table):
        widened = jnp.broadcast_to(
            slot_table[:, :, None, :], (slot_table.shape[0], EXPERTS, expert_span, CAP)
        )
        return widened.reshape(slot_table.shape[0], EXPERTS * expert_span * CAP)

    member_wide = spread(member)
    scaled_wide = spread(scaled)
    token_send = jnp.einsum(
        "tr,tc->rc", member_wide.astype(jnp.bfloat16), tokens, preferred_element_type=jnp.float32
    ).astype(jnp.bfloat16)
    grad_send = jnp.einsum(
        "tr,tc->rc", scaled_wide, cotangent.astype(jnp.float32), precision=precise
    ).astype(jnp.bfloat16)
    send = jnp.concatenate(
        [token_send.reshape(n_src, CAP, feature_cols), grad_send.reshape(n_src, CAP, feature_cols)],
        axis=1,
    )
    recv = lax.all_to_all(send, SRC, split_axis=0, concat_axis=0, tiled=True)
    mine = recv.reshape(n_src, 2, CAP, feature_cols).transpose(1, 0, 2, 3)
    mine = mine.reshape(2, n_src * CAP, feature_cols)
    mine_full = lax.all_gather(mine, TN, axis=2, tiled=True)
    pair = [(0, 1), (1, 0)]
    other_full = lax.ppermute(mine_full, "core", pair)

    gate_local = gate_matrix[0]
    up_local = up_matrix[0]
    down_local = down_matrix[0]

    def forward(rows):
        gate_pre = jnp.dot(rows, gate_local, preferred_element_type=jnp.float32)
        up_pre = jnp.dot(rows, up_local, preferred_element_type=jnp.float32)
        sigmoid_gate = jax.nn.sigmoid(gate_pre)
        activated = gate_pre * sigmoid_gate
        hidden = (activated * up_pre).astype(jnp.bfloat16)
        out_t = jnp.einsum(
            "hd,rh->dr", down_local, hidden, preferred_element_type=jnp.float32
        ).astype(jnp.bfloat16)
        out_t = with_layout_constraint(out_t, Layout(major_to_minor=(0, 1)))
        return gate_pre, up_pre, sigmoid_gate, activated, hidden, out_t

    def backward(grads, gate_pre, up_pre, sigmoid_gate, activated):
        hidden_grad = jnp.einsum(
            "rd,hd->rh", grads, down_local, preferred_element_type=jnp.float32
        )
        gate_grad = (
            hidden_grad * up_pre * sigmoid_gate * (1.0 + gate_pre * (1.0 - sigmoid_gate))
        ).astype(jnp.bfloat16)
        up_grad = (hidden_grad * activated).astype(jnp.bfloat16)
        back_t = (
            jnp.einsum("dh,rh->dr", gate_local, gate_grad, preferred_element_type=jnp.float32)
            + jnp.einsum("dh,rh->dr", up_local, up_grad, preferred_element_type=jnp.float32)
        ).astype(jnp.bfloat16)
        back_t = with_layout_constraint(back_t, Layout(major_to_minor=(0, 1)))
        return gate_grad, up_grad, back_t

    rows_a, grads_a = mine_full[0], mine_full[1]
    rows_b, grads_b = other_full[0], other_full[1]
    fa = forward(rows_a)
    ga, ua, back_a = backward(grads_a, *fa[:4])
    fb = forward(rows_b)
    gb, ub, back_b = backward(grads_b, *fb[:4])
    partner = lax.ppermute(jnp.concatenate([fb[5], back_b], axis=1), "core", pair)
    own = jnp.concatenate([fa[5], back_a], axis=1)
    summed = (own.astype(jnp.float32) + partner.astype(jnp.float32)).astype(jnp.bfloat16)
    scattered = lax.psum_scatter(summed, TN, scatter_dimension=0, tiled=True)
    n_rows = fa[5].shape[1]
    out_rows = scattered[:, :n_rows].T
    back_rows = scattered[:, n_rows:].T

    gate_gradient = (
        jnp.einsum("rd,rh->dh", rows_a, ga, preferred_element_type=jnp.float32)
        + jnp.einsum("rd,rh->dh", rows_b, gb, preferred_element_type=jnp.float32)
    ).astype(jnp.bfloat16)[None]
    up_gradient = (
        jnp.einsum("rd,rh->dh", rows_a, ua, preferred_element_type=jnp.float32)
        + jnp.einsum("rd,rh->dh", rows_b, ub, preferred_element_type=jnp.float32)
    ).astype(jnp.bfloat16)[None]
    down_gradient = (
        jnp.einsum("rh,rd->hd", fa[4], grads_a, preferred_element_type=jnp.float32)
        + jnp.einsum("rh,rd->hd", fb[4], grads_b, preferred_element_type=jnp.float32)
    ).astype(jnp.bfloat16)[None]

    done = jnp.concatenate(
        [
            out_rows.reshape(n_src, CAP, feature_cols),
            back_rows.reshape(n_src, CAP, feature_cols),
        ],
        axis=1,
    )
    returned = lax.all_to_all(done, SRC, split_axis=0, concat_axis=0, tiled=True).astype(
        jnp.float32
    )
    returned_out = returned[:, :CAP].reshape(-1, feature_cols)
    returned_back = returned[:, CAP:].reshape(-1, feature_cols)
    layer_out = jnp.dot(
        scaled_wide, returned_out, precision=precise, preferred_element_type=jnp.float32
    ).astype(jnp.bfloat16)
    token_gradient = jnp.dot(
        member_wide, returned_back, precision=precise, preferred_element_type=jnp.float32
    ).astype(jnp.bfloat16)
    return (layer_out, token_gradient, gate_gradient, up_gradient, down_gradient)


def solution(mesh):
    sizes = dict(mesh.shape)
    sub = Mesh(
        mesh.devices.reshape(
            sizes["dp"] // 4, 2, 2, 2, sizes["tensor"] // 2
        ),
        DP + TN,
    )
    in_specs = (
        P(DP, TN),
        P(DP, None),
        P(DP, None),
        P(DP, None, TN),
        P(DP, None, TN),
        P(DP, TN, None),
        P(DP, TN),
    )
    out_specs = (
        P(DP, TN),
        P(DP, TN),
        P(DP, None, TN),
        P(DP, None, TN),
        P(DP, TN, None),
    )
    placed = (
        P("dp", "tensor"),
        P("dp", "tensor"),
        P("dp", None, "tensor"),
        P("dp", None, "tensor"),
        P("dp", "tensor", None),
    )
    inner = jax.shard_map(
        per_device, mesh=sub, in_specs=in_specs, out_specs=out_specs, check_vma=False
    )

    def run(*args):
        outs = inner(*args)
        return tuple(
            lax.with_sharding_constraint(o, NamedSharding(mesh, p)) for o, p in zip(outs, placed)
        )

    return run
```

```python
import jax
import jax.numpy as jnp
from jax import lax
from jax.experimental.layout import Layout, with_layout_constraint
from jax.sharding import Mesh, NamedSharding, PartitionSpec as P

EXPERTS = 4
CAP = 32
DP = ("y", "xhi", "core")
TN = ("xlo", "z")
SRC = ("y", "xhi")


precise = lax.Precision.HIGHEST


def slot_tables(routes, gate_weights, capacity):
    experts = jnp.arange(EXPERTS, dtype=jnp.int32)
    hit_mask = routes[:, :, None] == experts[None, None, :]
    chosen = jnp.any(hit_mask, axis=1)
    weights = jnp.sum(
        jnp.where(hit_mask, gate_weights.astype(jnp.float32)[:, :, None], jnp.float32(0.0)), axis=1
    )
    places = jnp.cumsum(chosen.astype(jnp.int32), axis=0) - 1
    columns = jnp.arange(capacity, dtype=jnp.int32)
    onehot = (places[:, :, None] == columns[None, None, :]) & chosen[:, :, None]
    return (onehot, weights)


def per_device(tokens, routes, gate_weights, gate_matrix, up_matrix, down_matrix, cotangent):
    feature_cols = tokens.shape[1]
    n_src = lax.axis_size(SRC)
    expert_span = n_src // EXPERTS
    onehot, weights = slot_tables(routes, gate_weights, CAP)
    member = onehot.astype(jnp.float32)
    scaled = member * weights[:, :, None]

    def spread(slot_table):
        widened = jnp.broadcast_to(
            slot_table[:, :, None, :], (slot_table.shape[0], EXPERTS, expert_span, CAP)
        )
        return widened.reshape(slot_table.shape[0], EXPERTS * expert_span * CAP)

    member_wide = spread(member)
    scaled_wide = spread(scaled)
    token_send = jnp.einsum(
        "tr,tc->rc", member_wide.astype(jnp.bfloat16), tokens, preferred_element_type=jnp.float32
    ).astype(jnp.bfloat16)
    grad_send = jnp.einsum(
        "tr,tc->rc", scaled_wide, cotangent.astype(jnp.float32), precision=precise
    ).astype(jnp.bfloat16)
    send = jnp.concatenate(
        [token_send.reshape(n_src, CAP, feature_cols), grad_send.reshape(n_src, CAP, feature_cols)],
        axis=1,
    )
    recv = lax.all_to_all(send, SRC, split_axis=0, concat_axis=0, tiled=True)
    mine = recv.reshape(n_src, 2, CAP, feature_cols).transpose(1, 0, 2, 3)
    mine = mine.reshape(2, n_src * CAP, feature_cols)
    mine_full = lax.all_gather(mine, TN, axis=2, tiled=True)
    pair = [(0, 1), (1, 0)]

    gate_local = gate_matrix[0]
    up_local = up_matrix[0]
    down_local = down_matrix[0]
    gate_other, up_other, down_other = lax.ppermute(
        (gate_local, up_local, down_local), "core", pair
    )

    def forward(rows, gate_w, up_w, down_w):
        gate_pre = jnp.dot(rows, gate_w, preferred_element_type=jnp.float32)
        up_pre = jnp.dot(rows, up_w, preferred_element_type=jnp.float32)
        sigmoid_gate = jax.nn.sigmoid(gate_pre)
        activated = gate_pre * sigmoid_gate
        hidden = (activated * up_pre).astype(jnp.bfloat16)
        out_t = jnp.einsum(
            "hd,rh->dr", down_w, hidden, preferred_element_type=jnp.float32
        ).astype(jnp.bfloat16)
        out_t = with_layout_constraint(out_t, Layout(major_to_minor=(0, 1)))
        return gate_pre, up_pre, sigmoid_gate, activated, hidden, out_t

    def backward(grads, gate_pre, up_pre, sigmoid_gate, activated, gate_w, up_w, down_w):
        hidden_grad = jnp.einsum(
            "rd,hd->rh", grads, down_w, preferred_element_type=jnp.float32
        )
        gate_grad = (
            hidden_grad * up_pre * sigmoid_gate * (1.0 + gate_pre * (1.0 - sigmoid_gate))
        ).astype(jnp.bfloat16)
        up_grad = (hidden_grad * activated).astype(jnp.bfloat16)
        back_t = (
            jnp.einsum("dh,rh->dr", gate_w, gate_grad, preferred_element_type=jnp.float32)
            + jnp.einsum("dh,rh->dr", up_w, up_grad, preferred_element_type=jnp.float32)
        ).astype(jnp.bfloat16)
        back_t = with_layout_constraint(back_t, Layout(major_to_minor=(0, 1)))
        return gate_grad, up_grad, back_t

    rows, grads = mine_full[0], mine_full[1]
    own_w = (gate_local, up_local, down_local)
    other_w = (gate_other, up_other, down_other)
    f_own = forward(rows, *own_w)
    f_other = forward(rows, *other_w)
    b_own = backward(grads, *f_own[:4], *own_w)
    b_other = backward(grads, *f_other[:4], *other_w)
    own = jnp.concatenate([f_own[5], b_own[2]], axis=1)
    other = jnp.concatenate([f_other[5], b_other[2]], axis=1)
    summed = (own.astype(jnp.float32) + other.astype(jnp.float32)).astype(jnp.bfloat16)
    scattered = lax.psum_scatter(summed, TN, scatter_dimension=0, tiled=True)
    n_rows = f_own[5].shape[1]
    out_rows = scattered[:, :n_rows].T
    back_rows = scattered[:, n_rows:].T

    def weight_grads(f, b):
        return (
            jnp.einsum("rd,rh->dh", rows, b[0], preferred_element_type=jnp.float32),
            jnp.einsum("rd,rh->dh", rows, b[1], preferred_element_type=jnp.float32),
            jnp.einsum("rh,rd->hd", f[4], grads, preferred_element_type=jnp.float32),
        )

    w_own = weight_grads(f_own, b_own)
    w_recv = lax.ppermute(weight_grads(f_other, b_other), "core", pair)
    gate_gradient = (w_own[0] + w_recv[0]).astype(jnp.bfloat16)[None]
    up_gradient = (w_own[1] + w_recv[1]).astype(jnp.bfloat16)[None]
    down_gradient = (w_own[2] + w_recv[2]).astype(jnp.bfloat16)[None]

    done = jnp.concatenate(
        [
            out_rows.reshape(n_src, CAP, feature_cols),
            back_rows.reshape(n_src, CAP, feature_cols),
        ],
        axis=1,
    )
    returned = lax.all_to_all(done, SRC, split_axis=0, concat_axis=0, tiled=True).astype(
        jnp.float32
    )
    returned_out = returned[:, :CAP].reshape(-1, feature_cols)
    returned_back = returned[:, CAP:].reshape(-1, feature_cols)
    layer_out = jnp.dot(
        scaled_wide, returned_out, precision=precise, preferred_element_type=jnp.float32
    ).astype(jnp.bfloat16)
    token_gradient = jnp.dot(
        member_wide, returned_back, precision=precise, preferred_element_type=jnp.float32
    ).astype(jnp.bfloat16)
    return (layer_out, token_gradient, gate_gradient, up_gradient, down_gradient)


def solution(mesh):
    sizes = dict(mesh.shape)
    sub = Mesh(
        mesh.devices.reshape(
            sizes["dp"] // 4, 2, 2, 2, sizes["tensor"] // 2
        ),
        DP + TN,
    )
    in_specs = (
        P(DP, TN),
        P(DP, None),
        P(DP, None),
        P(DP, None, TN),
        P(DP, None, TN),
        P(DP, TN, None),
        P(DP, TN),
    )
    out_specs = (
        P(DP, TN),
        P(DP, TN),
        P(DP, None, TN),
        P(DP, None, TN),
        P(DP, TN, None),
    )
    placed = (
        P("dp", "tensor"),
        P("dp", "tensor"),
        P("dp", None, "tensor"),
        P("dp", None, "tensor"),
        P("dp", "tensor", None),
    )
    inner = jax.shard_map(
        per_device, mesh=sub, in_specs=in_specs, out_specs=out_specs, check_vma=False
    )

    def run(*args):
        outs = inner(*args)
        return tuple(
            lax.with_sharding_constraint(o, NamedSharding(mesh, p)) for o, p in zip(outs, placed)
        )

    return run
```

```python
import jax
import jax.numpy as jnp
from jax import lax
from jax.experimental.layout import Layout, with_layout_constraint
from jax.sharding import Mesh, NamedSharding, PartitionSpec as P

EXPERTS = 4
CAP = 32
DP = ("y", "xhi", "core")
TN = ("xlo", "z")
SRC = ("y", "xhi")


precise = lax.Precision.HIGHEST


def slot_tables(routes, gate_weights, capacity):
    experts = jnp.arange(EXPERTS, dtype=jnp.int32)
    hit_mask = routes[:, :, None] == experts[None, None, :]
    chosen = jnp.any(hit_mask, axis=1)
    weights = jnp.sum(
        jnp.where(hit_mask, gate_weights.astype(jnp.float32)[:, :, None], jnp.float32(0.0)), axis=1
    )
    places = jnp.cumsum(chosen.astype(jnp.int32), axis=0) - 1
    columns = jnp.arange(capacity, dtype=jnp.int32)
    onehot = (places[:, :, None] == columns[None, None, :]) & chosen[:, :, None]
    return (onehot, weights)


def per_device(tokens, routes, gate_weights, gate_matrix, up_matrix, down_matrix, cotangent):
    feature_cols = tokens.shape[1]
    n_src = lax.axis_size(SRC)
    expert_span = n_src // EXPERTS
    onehot, weights = slot_tables(routes, gate_weights, CAP)
    member = onehot.astype(jnp.float32)
    scaled = member * weights[:, :, None]

    def spread(slot_table):
        widened = jnp.broadcast_to(
            slot_table[:, :, None, :], (slot_table.shape[0], EXPERTS, expert_span, CAP)
        )
        return widened.reshape(slot_table.shape[0], EXPERTS * expert_span * CAP)

    member_wide = spread(member)
    scaled_wide = spread(scaled)
    token_send = jnp.einsum(
        "tr,tc->rc", member_wide.astype(jnp.bfloat16), tokens, preferred_element_type=jnp.float32
    ).astype(jnp.bfloat16)
    grad_send = jnp.einsum(
        "tr,tc->rc", scaled_wide, cotangent.astype(jnp.float32), precision=precise
    ).astype(jnp.bfloat16)
    send = jnp.concatenate(
        [token_send.reshape(n_src, CAP, feature_cols), grad_send.reshape(n_src, CAP, feature_cols)],
        axis=1,
    )
    recv = lax.all_to_all(send, SRC, split_axis=0, concat_axis=0, tiled=True)
    mine = recv.reshape(n_src, 2, CAP, feature_cols).transpose(1, 0, 2, 3)
    mine = mine.reshape(2, n_src * CAP, feature_cols)
    mine_full = lax.all_gather(mine, TN, axis=2, tiled=True)
    pair = [(0, 1), (1, 0)]

    gate_local = gate_matrix[0]
    up_local = up_matrix[0]
    down_local = down_matrix[0]
    gu_local = jnp.concatenate([gate_local, up_local], axis=1)
    gu_other, down_other = lax.ppermute((gu_local, down_local), "core", pair)

    def forward(rows, gu_w, down_w):
        pre = jnp.dot(rows, gu_w, preferred_element_type=jnp.float32)
        width = pre.shape[1] // 2
        gate_pre, up_pre = pre[:, :width], pre[:, width:]
        sigmoid_gate = jax.nn.sigmoid(gate_pre)
        activated = gate_pre * sigmoid_gate
        hidden = (activated * up_pre).astype(jnp.bfloat16)
        out_t = jnp.einsum(
            "hd,rh->dr", down_w, hidden, preferred_element_type=jnp.float32
        ).astype(jnp.bfloat16)
        out_t = with_layout_constraint(out_t, Layout(major_to_minor=(0, 1)))
        return gate_pre, up_pre, sigmoid_gate, activated, hidden, out_t

    def backward(grads, gate_pre, up_pre, sigmoid_gate, activated, gu_w, down_w):
        hidden_grad = jnp.einsum(
            "rd,hd->rh", grads, down_w, preferred_element_type=jnp.float32
        )
        gate_grad = (
            hidden_grad * up_pre * sigmoid_gate * (1.0 + gate_pre * (1.0 - sigmoid_gate))
        ).astype(jnp.bfloat16)
        up_grad = (hidden_grad * activated).astype(jnp.bfloat16)
        both_grad = jnp.concatenate([gate_grad, up_grad], axis=1)
        back_t = jnp.einsum(
            "dh,rh->dr", gu_w, both_grad, preferred_element_type=jnp.float32
        ).astype(jnp.bfloat16)
        back_t = with_layout_constraint(back_t, Layout(major_to_minor=(0, 1)))
        return gate_grad, up_grad, back_t

    rows, grads = mine_full[0], mine_full[1]
    own_w = (gu_local, down_local)
    other_w = (gu_other, down_other)
    f_own = forward(rows, *own_w)
    f_other = forward(rows, *other_w)
    b_own = backward(grads, *f_own[:4], *own_w)
    b_other = backward(grads, *f_other[:4], *other_w)
    own = jnp.concatenate([f_own[5], b_own[2]], axis=1)
    other = jnp.concatenate([f_other[5], b_other[2]], axis=1)
    summed = (own.astype(jnp.float32) + other.astype(jnp.float32)).astype(jnp.bfloat16)
    scattered = lax.psum_scatter(summed, TN, scatter_dimension=0, tiled=True)
    n_rows = f_own[5].shape[1]
    out_rows = scattered[:, :n_rows].T
    back_rows = scattered[:, n_rows:].T

    def weight_grads(f, b):
        return (
            jnp.einsum("rd,rh->dh", rows, b[0], preferred_element_type=jnp.float32),
            jnp.einsum("rd,rh->dh", rows, b[1], preferred_element_type=jnp.float32),
            jnp.einsum("rh,rd->hd", f[4], grads, preferred_element_type=jnp.float32),
        )

    w_own = weight_grads(f_own, b_own)
    w_recv = lax.ppermute(weight_grads(f_other, b_other), "core", pair)
    gate_gradient = (w_own[0] + w_recv[0]).astype(jnp.bfloat16)[None]
    up_gradient = (w_own[1] + w_recv[1]).astype(jnp.bfloat16)[None]
    down_gradient = (w_own[2] + w_recv[2]).astype(jnp.bfloat16)[None]

    done = jnp.concatenate(
        [
            out_rows.reshape(n_src, CAP, feature_cols),
            back_rows.reshape(n_src, CAP, feature_cols),
        ],
        axis=1,
    )
    returned = lax.all_to_all(done, SRC, split_axis=0, concat_axis=0, tiled=True).astype(
        jnp.float32
    )
    returned_out = returned[:, :CAP].reshape(-1, feature_cols)
    returned_back = returned[:, CAP:].reshape(-1, feature_cols)
    layer_out = jnp.dot(
        scaled_wide, returned_out, precision=precise, preferred_element_type=jnp.float32
    ).astype(jnp.bfloat16)
    token_gradient = jnp.dot(
        member_wide, returned_back, precision=precise, preferred_element_type=jnp.float32
    ).astype(jnp.bfloat16)
    return (layer_out, token_gradient, gate_gradient, up_gradient, down_gradient)


def solution(mesh):
    sizes = dict(mesh.shape)
    sub = Mesh(
        mesh.devices.reshape(
            sizes["dp"] // 4, 2, 2, 2, sizes["tensor"] // 2
        ),
        DP + TN,
    )
    in_specs = (
        P(DP, TN),
        P(DP, None),
        P(DP, None),
        P(DP, None, TN),
        P(DP, None, TN),
        P(DP, TN, None),
        P(DP, TN),
    )
    out_specs = (
        P(DP, TN),
        P(DP, TN),
        P(DP, None, TN),
        P(DP, None, TN),
        P(DP, TN, None),
    )
    placed = (
        P("dp", "tensor"),
        P("dp", "tensor"),
        P("dp", None, "tensor"),
        P("dp", None, "tensor"),
        P("dp", "tensor", None),
    )
    inner = jax.shard_map(
        per_device, mesh=sub, in_specs=in_specs, out_specs=out_specs, check_vma=False
    )

    def run(*args):
        outs = inner(*args)
        return tuple(
            lax.with_sharding_constraint(o, NamedSharding(mesh, p)) for o, p in zip(outs, placed)
        )

    return run
```

```python
import jax
import jax.numpy as jnp
from jax import lax
from jax.experimental.layout import Layout, with_layout_constraint
from jax.sharding import Mesh, NamedSharding, PartitionSpec as P

EXPERTS = 4
CAP = 32
DP = ("y", "xhi", "core")
TN = ("xlo", "z")
SRC = ("y", "xhi")


precise = lax.Precision.HIGHEST


def slot_tables(routes, gate_weights, capacity):
    experts = jnp.arange(EXPERTS, dtype=jnp.int32)
    hit_mask = routes[:, :, None] == experts[None, None, :]
    chosen = jnp.any(hit_mask, axis=1)
    weights = jnp.sum(
        jnp.where(hit_mask, gate_weights.astype(jnp.float32)[:, :, None], jnp.float32(0.0)), axis=1
    )
    places = jnp.cumsum(chosen.astype(jnp.int32), axis=0) - 1
    columns = jnp.arange(capacity, dtype=jnp.int32)
    onehot = (places[:, :, None] == columns[None, None, :]) & chosen[:, :, None]
    return (onehot, weights)


def per_device(tokens, routes, gate_weights, gate_matrix, up_matrix, down_matrix, cotangent):
    feature_cols = tokens.shape[1]
    n_src = lax.axis_size(SRC)
    expert_span = n_src // EXPERTS
    onehot, weights = slot_tables(routes, gate_weights, CAP)
    member = onehot.astype(jnp.float32)
    scaled = member * weights[:, :, None]

    def spread(slot_table):
        widened = jnp.broadcast_to(
            slot_table[:, :, None, :], (slot_table.shape[0], EXPERTS, expert_span, CAP)
        )
        return widened.reshape(slot_table.shape[0], EXPERTS * expert_span * CAP)

    member_wide = spread(member)
    scaled_wide = spread(scaled)
    token_send = jnp.einsum(
        "tr,tc->rc", member_wide.astype(jnp.bfloat16), tokens, preferred_element_type=jnp.float32
    ).astype(jnp.bfloat16)
    grad_send = jnp.einsum(
        "tr,tc->rc", scaled_wide, cotangent.astype(jnp.float32), precision=precise
    ).astype(jnp.bfloat16)
    send = jnp.concatenate(
        [token_send.reshape(n_src, CAP, feature_cols), grad_send.reshape(n_src, CAP, feature_cols)],
        axis=1,
    )
    recv = lax.all_to_all(send, SRC, split_axis=0, concat_axis=0, tiled=True)
    mine = recv.reshape(n_src, 2, CAP, feature_cols).transpose(1, 0, 2, 3)
    mine = mine.reshape(2, n_src * CAP, feature_cols)
    mine_full = lax.all_gather(mine, TN, axis=2, tiled=True)
    pair = [(0, 1), (1, 0)]

    gate_local = gate_matrix[0]
    up_local = up_matrix[0]
    down_local = down_matrix[0]
    gu_local = jnp.concatenate([gate_local, up_local], axis=1)
    gu_other, down_other = lax.ppermute((gu_local, down_local), "core", pair)

    def forward(pre, gu_w, down_w):
        width = pre.shape[1] // 2
        gate_pre, up_pre = pre[:, :width], pre[:, width:]
        sigmoid_gate = jax.nn.sigmoid(gate_pre)
        activated = gate_pre * sigmoid_gate
        hidden = (activated * up_pre).astype(jnp.bfloat16)
        out_t = jnp.einsum(
            "hd,rh->dr", down_w, hidden, preferred_element_type=jnp.float32
        ).astype(jnp.bfloat16)
        out_t = with_layout_constraint(out_t, Layout(major_to_minor=(0, 1)))
        return gate_pre, up_pre, sigmoid_gate, activated, hidden, out_t

    def backward(hidden_grad, gate_pre, up_pre, sigmoid_gate, activated, gu_w, down_w):
        gate_grad = (
            hidden_grad * up_pre * sigmoid_gate * (1.0 + gate_pre * (1.0 - sigmoid_gate))
        ).astype(jnp.bfloat16)
        up_grad = (hidden_grad * activated).astype(jnp.bfloat16)
        both_grad = jnp.concatenate([gate_grad, up_grad], axis=1)
        back_t = jnp.einsum(
            "dh,rh->dr", gu_w, both_grad, preferred_element_type=jnp.float32
        ).astype(jnp.bfloat16)
        back_t = with_layout_constraint(back_t, Layout(major_to_minor=(0, 1)))
        return gate_grad, up_grad, back_t

    rows, grads = mine_full[0], mine_full[1]
    own_w = (gu_local, down_local)
    other_w = (gu_other, down_other)
    width = gu_local.shape[1]
    pre_both = jnp.dot(
        rows, jnp.concatenate([gu_local, gu_other], axis=1), preferred_element_type=jnp.float32
    )
    hgrad_both = jnp.einsum(
        "rd,hd->rh",
        grads,
        jnp.concatenate([down_local, down_other], axis=0),
        preferred_element_type=jnp.float32,
    )
    f_own = forward(pre_both[:, :width], *own_w)
    f_other = forward(pre_both[:, width:], *other_w)
    b_own = backward(hgrad_both[:, : width // 2], *f_own[:4], *own_w)
    b_other = backward(hgrad_both[:, width // 2 :], *f_other[:4], *other_w)
    own = jnp.concatenate([f_own[5], b_own[2]], axis=1)
    other = jnp.concatenate([f_other[5], b_other[2]], axis=1)
    summed = (own.astype(jnp.float32) + other.astype(jnp.float32)).astype(jnp.bfloat16)
    scattered = lax.psum_scatter(summed, TN, scatter_dimension=0, tiled=True)
    n_rows = f_own[5].shape[1]
    out_rows = scattered[:, :n_rows].T
    back_rows = scattered[:, n_rows:].T

    def weight_grads(f, b):
        return (
            jnp.einsum("rd,rh->dh", rows, b[0], preferred_element_type=jnp.float32),
            jnp.einsum("rd,rh->dh", rows, b[1], preferred_element_type=jnp.float32),
            jnp.einsum("rh,rd->hd", f[4], grads, preferred_element_type=jnp.float32),
        )

    w_own = weight_grads(f_own, b_own)
    w_recv = lax.ppermute(weight_grads(f_other, b_other), "core", pair)
    gate_gradient = (w_own[0] + w_recv[0]).astype(jnp.bfloat16)[None]
    up_gradient = (w_own[1] + w_recv[1]).astype(jnp.bfloat16)[None]
    down_gradient = (w_own[2] + w_recv[2]).astype(jnp.bfloat16)[None]

    done = jnp.concatenate(
        [
            out_rows.reshape(n_src, CAP, feature_cols),
            back_rows.reshape(n_src, CAP, feature_cols),
        ],
        axis=1,
    )
    returned = lax.all_to_all(done, SRC, split_axis=0, concat_axis=0, tiled=True).astype(
        jnp.float32
    )
    returned_out = returned[:, :CAP].reshape(-1, feature_cols)
    returned_back = returned[:, CAP:].reshape(-1, feature_cols)
    layer_out = jnp.dot(
        scaled_wide, returned_out, precision=precise, preferred_element_type=jnp.float32
    ).astype(jnp.bfloat16)
    token_gradient = jnp.dot(
        member_wide, returned_back, precision=precise, preferred_element_type=jnp.float32
    ).astype(jnp.bfloat16)
    return (layer_out, token_gradient, gate_gradient, up_gradient, down_gradient)


def solution(mesh):
    sizes = dict(mesh.shape)
    sub = Mesh(
        mesh.devices.reshape(
            sizes["dp"] // 4, 2, 2, 2, sizes["tensor"] // 2
        ),
        DP + TN,
    )
    in_specs = (
        P(DP, TN),
        P(DP, None),
        P(DP, None),
        P(DP, None, TN),
        P(DP, None, TN),
        P(DP, TN, None),
        P(DP, TN),
    )
    out_specs = (
        P(DP, TN),
        P(DP, TN),
        P(DP, None, TN),
        P(DP, None, TN),
        P(DP, TN, None),
    )
    placed = (
        P("dp", "tensor"),
        P("dp", "tensor"),
        P("dp", None, "tensor"),
        P("dp", None, "tensor"),
        P("dp", "tensor", None),
    )
    inner = jax.shard_map(
        per_device, mesh=sub, in_specs=in_specs, out_specs=out_specs, check_vma=False
    )

    def run(*args):
        outs = inner(*args)
        return tuple(
            lax.with_sharding_constraint(o, NamedSharding(mesh, p)) for o, p in zip(outs, placed)
        )

    return run
```
